256 devices in a mesh: feeder: 32 (over z_hi, y, core), factor: 8 (over z_lo, x).
Axes of the slice: x: 4, y: 4, z: 8 (z_hi: 4, z_lo: 2; z = z_hi * 2 + z_lo), core: 2. Of those that a mesh axis runs over, the one named last changes fastest.
Arguments:
- sensitivity: bfloat16 [32, 2048, 2048], P('feeder'), may hold values from -0.015625 to 0.015625
- headroom: float32 [32, 8, 2048], P('feeder'), may hold values from 0 to 3
- ev_power: float32 [32, 8, 256], P('feeder'), may hold values from 0.5 to 4
- ev_node: int32 [32, 8, 256], P('feeder'), may hold values from 0 to 2047
- region_map: int32 [32, 256], P('feeder'), may hold values from 0 to 511
- loadings: float32 [512, 8, 512], P('feeder', None, 'factor'), may hold values from -8 to 8
Outputs:
- margin: float32 [32, 8, 2048], P('feeder')
- new_loadings: float32 [512, 8, 512], P('feeder', None, 'factor')
The draws below stay inside these ranges and needn't reach their ends.
All inputs are finite; a program needn't handle non-finite values.
Results may differ from the reference program's by a relative error of at most 0.0031.
Values may be sent and summed in bfloat16 or wider, within the bound.
No kernel may reach another device: no remote copies, remote signals or barrier semaphores. Data moves between devices by JAX's collectives and lax.ppermute only.
A program may use at most 64 MiB of HBM per device.

```python
import math
import jax
import jax.numpy as jnp
from jax import lax

NODES = 2048
RANK = 512
INTERVALS = 8
EVS = 256
FEEDERS = 32
REGIONS = 512


def draw_loadings(key, part):
    first_key = jax.random.fold_in(key, 11)
    column = jnp.arange(RANK, dtype=jnp.float32) / float(max(RANK - 1, 1))
    values = jax.random.normal(first_key, (REGIONS, INTERVALS, RANK), jnp.float32)
    values = values * (3.0 ** column / 1.9)[None, None, :]
    return jnp.clip(values, -8.0, 8.0).astype(jnp.float32)


def with_ends(values, own_key, low, high):
    index_at = [jax.random.randint(jax.random.fold_in(own_key, axis), (), 0, length) for axis, length in enumerate(values.shape)]
    longest = values.shape.index(max(values.shape))
    next_to = index_at[:longest] + [(index_at[longest] + 1) % values.shape[longest]] + index_at[longest + 1:]
    return values.at[tuple(index_at)].set(low).at[tuple(next_to)].set(high)


def block_scale(stream_key, shape, pieces, least, top_value):
    level = 1.0
    for axis_at, blocks in pieces:
        heights = jax.random.uniform(jax.random.fold_in(jax.random.fold_in(stream_key, 6), axis_at), (blocks,), jnp.float32, least / len(pieces), top_value / len(pieces))
        level = level * jnp.repeat(jnp.exp(heights), shape[axis_at] // blocks).reshape((-1,) + (1,) * (len(shape) - 1 - axis_at))
    return level


def gaussian(key, extent, scale, limit, cuts=(), kind=jnp.bfloat16):
    drawn = jax.random.normal(key, extent, jnp.float32) * scale
    if len(cuts) > 0:
        drawn = block_scale(key, extent, cuts, -0.22, 0.18) * drawn
    return jnp.clip(drawn, min=-limit, max=limit).astype(kind)


def setup_inputs(seed: int = 0) -> dict:
    seeds = jax.random.split(jax.random.key(seed), 7)
    sensitivity = gaussian(seeds[0], (FEEDERS, NODES, NODES), (EVS * RANK) ** -0.5, 0.015625, ((0, 32),))
    headroom = jnp.clip(3.0 * jax.random.uniform(seeds[1], (FEEDERS, INTERVALS, NODES), jnp.float32) ** block_scale(seeds[1], (FEEDERS, INTERVALS, NODES), ((0, 32),), -0.2, 0.2), 0.0, 3.0)
    ev_power = jnp.clip(jnp.exp(math.log(4.0) - 2.0794415 * jax.random.uniform(seeds[2], (FEEDERS, INTERVALS, EVS), jnp.float32) ** block_scale(seeds[2], (FEEDERS, INTERVALS, EVS), ((0, 32),), -0.2, 0.2)), 0.5, 4.0)
    ev_node = with_ends(jax.random.randint(seeds[3], (FEEDERS, INTERVALS, EVS), 0, NODES), jax.random.fold_in(seeds[3], 1), 0, NODES - 1).astype(jnp.int32)
    region_map = with_ends(jax.random.randint(seeds[4], (FEEDERS, EVS), 0, REGIONS), jax.random.fold_in(seeds[4], 1), 0, REGIONS - 1).astype(jnp.int32)
    loadings = draw_loadings(jax.random.fold_in(seeds[6], 71), 0)
    return {"sensitivity": sensitivity, "headroom": headroom, "ev_power": ev_power, "ev_node": ev_node, "region_map": region_map, "loadings": loadings}


quantile = 1.645
epsilon = 1e-06
step_size = 16.0

def reference(sensitivity, headroom, ev_power, ev_node, region_map, loadings):
    rounded = loadings.astype(jnp.bfloat16)

    def per_feeder(grad_total, inputs):
        sens_block, room, power, nodes, regions = inputs
        looked = rounded[regions].astype(jnp.float32)
        volts_list = []
        rows_list = []
        variance_list = []
        for interval in range(INTERVALS):
            weighted = (power[interval][:, None] * looked[:, interval, :]).astype(jnp.bfloat16)
            sens_rows = sens_block[nodes[interval]]
            factor_volts = jnp.dot(weighted.T, sens_rows, preferred_element_type=jnp.float32)
            volts_list.append(factor_volts)
            rows_list.append(sens_rows)
            variance_list.append(lax.optimization_barrier(jnp.sum(factor_volts * factor_volts, axis=0)))
        variance = jnp.stack(variance_list, axis=0)
        deviation = jnp.sqrt(variance + epsilon)
        margin = room - quantile * deviation
        violation = jnp.maximum(-margin, 0.0)
        var_grad = quantile * violation / deviation
        grads = []
        for interval in range(INTERVALS):
            volt_grad = (2.0 * var_grad[interval][None, :] * volts_list[interval]).astype(jnp.bfloat16)
            weight_grad = jnp.dot(rows_list[interval], volt_grad.T, preferred_element_type=jnp.float32)
            grads.append(power[interval][:, None] * weight_grad)
        load_grad = jnp.stack(grads, axis=1)
        grad_total = grad_total + jax.ops.segment_sum(load_grad, regions, num_segments=REGIONS)
        return (grad_total, margin)
    initial = jnp.zeros((REGIONS, INTERVALS, RANK), jnp.float32)
    grad_total, margins = lax.scan(per_feeder, initial, (sensitivity, headroom, ev_power, ev_node, region_map))
    return (margins, loadings - step_size * grad_total)
```

```python
import jax
import jax.numpy as jnp
from jax import lax
from jax.sharding import PartitionSpec as P

quantile = 1.645
epsilon = 1e-06
step_size = 16.0


def _bit_count(size):
    bits = size.bit_length() - 1
    assert (1 << bits) == size
    return bits


def _exchange(x, axis, bit, size):
    perm = [(i, i ^ (1 << bit)) for i in range(size)]
    return lax.ppermute(x, axis, perm)


def gather_blocks(x, axis):
    size = lax.axis_size(axis)
    bits = _bit_count(size)
    me = lax.axis_index(axis)
    buf = x
    for step, bit in enumerate(reversed(range(bits))):
        other = _exchange(buf, axis, bit, size)
        mine = (me >> bit) & 1
        low = jnp.where(mine == 0, buf, other)
        high = jnp.where(mine == 0, other, buf)
        buf = jnp.stack([low, high], axis=step)
    return buf.reshape((size * x.shape[0],) + x.shape[1:])


def scatter_blocks(x, axis):
    size = lax.axis_size(axis)
    bits = _bit_count(size)
    me = lax.axis_index(axis)
    block = x.shape[0] // size
    buf = x.reshape((2,) * bits + (block,) + x.shape[1:])
    for bit in range(bits):
        at = bits - 1 - bit
        mine = (me >> bit) & 1
        keep = lax.dynamic_index_in_dim(buf, mine, at, keepdims=False)
        send = lax.dynamic_index_in_dim(buf, 1 - mine, at, keepdims=False)
        buf = keep + _exchange(send, axis, bit, size)
    return buf


def sum_all(x, axis):
    size = lax.axis_size(axis)
    for bit in range(_bit_count(size)):
        x = x + _exchange(x, axis, bit, size)
    return x


def shards(sensitivity, headroom, ev_power, ev_node, region_map, loadings):
    reg_local, hours, columns = loadings.shape
    nodes = sensitivity.shape[2]
    ev_count = ev_power.shape[2]
    total_regions = reg_local * lax.axis_size("feeder")
    packed = loadings.astype(jnp.bfloat16).reshape(reg_local, hours * columns)
    shard_rows = gather_blocks(packed, "feeder")
    regions = region_map.reshape(-1)
    matches = (regions[:, None] == lax.iota(jnp.int32, total_regions)[None, :]).astype(jnp.bfloat16)
    looked = jnp.dot(matches, shard_rows, preferred_element_type=jnp.float32)
    looked = looked.reshape(ev_count, hours, columns)
    power = ev_power[0].T
    weighted = (power[:, :, None] * looked).astype(jnp.bfloat16)
    node_hot = (ev_node[0][:, :, None] == lax.iota(jnp.int32, nodes)[None, None, :]).astype(jnp.bfloat16)
    spread = jnp.einsum("hkm,khr->mhr", node_hot, weighted, preferred_element_type=jnp.float32)
    spread_hi = spread.astype(jnp.bfloat16)
    spread_lo = (spread - spread_hi.astype(jnp.float32)).astype(jnp.bfloat16)
    both = jnp.concatenate([spread_hi, spread_lo], axis=2)
    sens = sensitivity[0]
    volts_both = jnp.einsum("mhr,mn->hrn", both, sens, preferred_element_type=jnp.float32)
    factor_volts = volts_both[:, :columns] + volts_both[:, columns:]
    partial_sum = jnp.sum(factor_volts * factor_volts, axis=1)
    variance = sum_all(partial_sum, "factor")[None]
    deviation = jnp.sqrt(variance + epsilon)
    margin = headroom - quantile * deviation
    violation = jnp.maximum(-margin, 0.0)
    var_grad = quantile * violation / deviation
    volt_grad = (2.0 * var_grad[0][:, None, :] * factor_volts).astype(jnp.bfloat16)
    node_grads = jnp.einsum("mn,hrn->mhr", sens, volt_grad, preferred_element_type=jnp.float32)
    picked = jnp.einsum(
        "hkm,mhr->khr",
        node_hot,
        node_grads,
        precision=lax.Precision.HIGHEST,
        preferred_element_type=jnp.float32,
    )
    member_grads = (power[:, :, None] * picked).reshape(ev_count, hours * columns)
    summed = jax.ops.segment_sum(member_grads, regions, num_segments=total_regions)
    reduced = scatter_blocks(summed, "feeder")
    new_loadings = loadings - step_size * reduced.reshape(reg_local, hours, columns)
    return (margin, new_loadings)


def solution(mesh):
    return jax.shard_map(
        shards,
        mesh=mesh,
        in_specs=(
            P("feeder", None, None),
            P("feeder", None, None),
            P("feeder", None, None),
            P("feeder", None, None),
            P("feeder", None),
            P("feeder", None, "factor"),
        ),
        out_specs=(P("feeder", None, None), P("feeder", None, "factor")),
        check_vma=False,
    )
```

```python
import jax
import jax.numpy as jnp
from jax import lax
from jax.sharding import PartitionSpec as P

quantile = 1.645
epsilon = 1e-06
step_size = 16.0


def _bit_count(size):
    bits = size.bit_length() - 1
    assert (1 << bits) == size
    return bits


def _exchange(x, axis, bit, size):
    perm = [(i, i ^ (1 << bit)) for i in range(size)]
    return lax.ppermute(x, axis, perm)


def gather_blocks(x, axis):
    size = lax.axis_size(axis)
    bits = _bit_count(size)
    me = lax.axis_index(axis)
    buf = x
    for step, bit in enumerate(reversed(range(bits))):
        other = _exchange(buf, axis, bit, size)
        mine = (me >> bit) & 1
        low = jnp.where(mine == 0, buf, other)
        high = jnp.where(mine == 0, other, buf)
        buf = jnp.stack([low, high], axis=step)
    return buf.reshape((size * x.shape[0],) + x.shape[1:])


def scatter_blocks(x, axis):
    size = lax.axis_size(axis)
    bits = _bit_count(size)
    me = lax.axis_index(axis)
    block = x.shape[0] // size
    buf = x.reshape((2,) * bits + (block,) + x.shape[1:])
    for bit in range(bits):
        at = bits - 1 - bit
        mine = (me >> bit) & 1
        keep = lax.dynamic_index_in_dim(buf, mine, at, keepdims=False)
        send = lax.dynamic_index_in_dim(buf, 1 - mine, at, keepdims=False)
        buf = keep + _exchange(send, axis, bit, size)
    return buf


def sum_all(x, axis):
    size = lax.axis_size(axis)
    for bit in range(_bit_count(size)):
        x = x + _exchange(x, axis, bit, size)
    return x


CHUNKS = 2


def _split_bf16(x):
    high = x.astype(jnp.bfloat16)
    low = (x - high.astype(jnp.float32)).astype(jnp.bfloat16)
    return high, low


def shards(sensitivity, headroom, ev_power, ev_node, region_map, loadings):
    reg_local, hours, columns = loadings.shape
    nodes = sensitivity.shape[2]
    ev_count = ev_power.shape[2]
    total_regions = reg_local * lax.axis_size("feeder")
    packed = loadings.astype(jnp.bfloat16).reshape(reg_local, hours * columns)
    shard_rows = gather_blocks(packed, "feeder")
    regions = region_map.reshape(-1)
    matches = (regions[:, None] == lax.iota(jnp.int32, total_regions)[None, :]).astype(jnp.bfloat16)
    looked = jnp.dot(matches, shard_rows, preferred_element_type=jnp.float32)
    looked = looked.reshape(ev_count, hours, columns)
    power = ev_power[0].T
    weighted = (power[:, :, None] * looked).astype(jnp.bfloat16)
    sens = sensitivity[0]
    span = hours // CHUNKS
    margins = []
    steps = []
    for chunk in range(CHUNKS):
        at = slice(chunk * span, (chunk + 1) * span)
        node_hot = (ev_node[0, at][:, :, None] == lax.iota(jnp.int32, nodes)[None, None, :]).astype(jnp.bfloat16)
        spread = jnp.einsum("hkm,khr->mhr", node_hot, weighted[:, at], preferred_element_type=jnp.float32)
        both = jnp.concatenate(_split_bf16(spread), axis=2)
        volts_both = jnp.einsum("mhr,mn->hrn", both, sens, preferred_element_type=jnp.float32)
        factor_volts = volts_both[:, :columns] + volts_both[:, columns:]
        partial_sum = jnp.sum(factor_volts * factor_volts, axis=1)
        variance = sum_all(partial_sum, "factor")
        deviation = jnp.sqrt(variance + epsilon)
        margin = headroom[0, at] - quantile * deviation
        violation = jnp.maximum(-margin, 0.0)
        var_grad = quantile * violation / deviation
        volt_grad = (2.0 * var_grad[:, None, :] * factor_volts).astype(jnp.bfloat16)
        node_grads = jnp.einsum("mn,hrn->mhr", sens, volt_grad, preferred_element_type=jnp.float32)
        grads_hi, grads_lo = _split_bf16(node_grads)
        picked = jnp.einsum("hkm,mhr->khr", node_hot, grads_hi, preferred_element_type=jnp.float32)
        picked = picked + jnp.einsum("hkm,mhr->khr", node_hot, grads_lo, preferred_element_type=jnp.float32)
        member_grads = (power[:, at, None] * picked).reshape(ev_count, span * columns)
        summed = jax.ops.segment_sum(member_grads, regions, num_segments=total_regions)
        reduced = scatter_blocks(summed, "feeder")
        margins.append(margin)
        steps.append(reduced.reshape(reg_local, span, columns))
    margin = jnp.concatenate(margins, axis=0)[None]
    new_loadings = loadings - step_size * jnp.concatenate(steps, axis=1)
    return (margin, new_loadings)


def solution(mesh):
    return jax.shard_map(
        shards,
        mesh=mesh,
        in_specs=(
            P("feeder", None, None),
            P("feeder", None, None),
            P("feeder", None, None),
            P("feeder", None, None),
            P("feeder", None),
            P("feeder", None, "factor"),
        ),
        out_specs=(P("feeder", None, None), P("feeder", None, "factor")),
        check_vma=False,
    )
```

```python
import jax
import jax.numpy as jnp
from jax import lax
from jax.sharding import PartitionSpec as P

quantile = 1.645
epsilon = 1e-06
step_size = 16.0


def _bit_count(size):
    bits = size.bit_length() - 1
    assert (1 << bits) == size
    return bits


def _exchange(x, axis, bit, size):
    perm = [(i, i ^ (1 << bit)) for i in range(size)]
    return lax.ppermute(x, axis, perm)


def gather_blocks(x, axis):
    size = lax.axis_size(axis)
    bits = _bit_count(size)
    me = lax.axis_index(axis)
    buf = x
    for step, bit in enumerate(reversed(range(bits))):
        other = _exchange(buf, axis, bit, size)
        mine = (me >> bit) & 1
        low = jnp.where(mine == 0, buf, other)
        high = jnp.where(mine == 0, other, buf)
        buf = jnp.stack([low, high], axis=step)
    return buf.reshape((size * x.shape[0],) + x.shape[1:])


def scatter_blocks(x, axis):
    size = lax.axis_size(axis)
    bits = _bit_count(size)
    me = lax.axis_index(axis)
    block = x.shape[0] // size
    buf = x.reshape((2,) * bits + (block,) + x.shape[1:])
    for bit in range(bits):
        at = bits - 1 - bit
        mine = (me >> bit) & 1
        keep = lax.dynamic_index_in_dim(buf, mine, at, keepdims=False)
        send = lax.dynamic_index_in_dim(buf, 1 - mine, at, keepdims=False)
        buf = keep + _exchange(send, axis, bit, size)
    return buf


def sum_all(x, axis):
    size = lax.axis_size(axis)
    for bit in range(_bit_count(size)):
        x = x + _exchange(x, axis, bit, size)
    return x


def _mask(j, bits):
    m = 0
    for pos, b in enumerate(bits):
        if (j >> pos) & 1:
            m |= 1 << b
    return m

def _sub(me, bits):
    s = 0
    for pos, b in enumerate(bits):
        s = s + ((me >> b) & 1) * (1 << pos)
    return s

def _send_all(x_for, axis, bits, size):
    out = {}
    for j in range(1, 1 << len(bits)):
        m = _mask(j, bits)
        out[j] = lax.ppermute(x_for(j), axis, [(i, i ^ m) for i in range(size)])
    return out

def _ordered(own, got, s, count):
    cand = jnp.stack([own] + [got[j] for j in range(1, count)])
    idx = jnp.arange(count, dtype=jnp.int32) ^ s
    return jnp.take(cand, idx, axis=0)

def gather_groups(x, axis, groups):
    size = lax.axis_size(axis)
    me = lax.axis_index(axis)
    buf = x[None]
    done = []
    for bits in groups:
        count = 1 << len(bits)
        s = _sub(me, bits)
        got = _send_all(lambda j: buf, axis, bits, size)
        stacked = _ordered(buf, got, s, count)
        buf = stacked
        done.append(bits)
    buf = buf.reshape(buf.shape[:len(groups)] + x.shape)
    order = sorted(range(len(groups)), key=lambda g: -max(groups[len(groups) - 1 - g]))
    buf = jnp.transpose(buf, order + list(range(len(groups), buf.ndim)))
    return buf.reshape((size * x.shape[0],) + x.shape[1:])

def scatter_groups(x, axis, groups):
    size = lax.axis_size(axis)
    me = lax.axis_index(axis)
    block = x.shape[0] // size
    total = sum(len(b) for b in groups)
    buf = x.reshape((2,) * total + (block,) + x.shape[1:])
    remaining = list(reversed(range(total)))
    for bits in groups:
        count = 1 << len(bits)
        s = _sub(me, bits)
        axes = [remaining.index(b) for b in reversed(bits)]
        rest = [a for a in range(len(remaining)) if a not in axes]
        buf = jnp.transpose(buf, axes + rest + list(range(len(remaining), buf.ndim)))
        buf = buf.reshape((count,) + buf.shape[len(bits):])
        remaining = [b for b in remaining if b not in bits]
        own = lax.dynamic_index_in_dim(buf, s, 0, keepdims=False)
        got = _send_all(lambda j: lax.dynamic_index_in_dim(buf, s ^ j, 0, keepdims=False), axis, bits, size)
        acc = own
        for j in range(1, count):
            acc = acc + got[j]
        buf = acc
    return buf

def sum_groups(x, axis, groups):
    size = lax.axis_size(axis)
    me = lax.axis_index(axis)
    for bits in groups:
        count = 1 << len(bits)
        s = _sub(me, bits)
        got = _send_all(lambda j: x, axis, bits, size)
        vals = _ordered(x, got, s, count)
        while vals.shape[0] > 1:
            vals = vals[0::2] + vals[1::2]
        x = vals[0]
    return x


def _bit_groups(axis):
    rest = list(range(1, _bit_count(lax.axis_size(axis))))
    pairs = [tuple(rest[max(0, i - 1) : i + 1]) for i in range(len(rest) - 1, -1, -2)]
    return pairs + [(0,)]


def _split_bf16(x):
    high = lax.reduce_precision(x, exponent_bits=8, mantissa_bits=7)
    return high.astype(jnp.bfloat16), (x - high).astype(jnp.bfloat16)


def shards(sensitivity, headroom, ev_power, ev_node, region_map, loadings):
    reg_local, hours, columns = loadings.shape
    nodes = sensitivity.shape[2]
    ev_count = ev_power.shape[2]
    total_regions = reg_local * lax.axis_size("feeder")
    packed = loadings.astype(jnp.bfloat16).reshape(reg_local, hours * columns)
    shard_rows = gather_groups(packed, "feeder", _bit_groups("feeder"))
    regions = region_map.reshape(-1)
    matches = (regions[:, None] == lax.iota(jnp.int32, total_regions)[None, :]).astype(jnp.bfloat16)
    looked = jnp.dot(matches, shard_rows, preferred_element_type=jnp.float32)
    looked = looked.reshape(ev_count, hours, columns)
    power = ev_power[0].T
    weighted = (power[:, :, None] * looked).astype(jnp.bfloat16)
    node_hot = (ev_node[0][:, :, None] == lax.iota(jnp.int32, nodes)[None, None, :]).astype(jnp.bfloat16)
    spread = jnp.einsum("hkm,khr->mhr", node_hot, weighted, preferred_element_type=jnp.float32)
    both = jnp.concatenate(_split_bf16(spread), axis=2)
    sens = sensitivity[0]
    volts_both = jnp.einsum("mhr,mn->hrn", both, sens, preferred_element_type=jnp.float32)
    factor_volts = volts_both[:, :columns] + volts_both[:, columns:]
    partial_sum = jnp.sum(factor_volts * factor_volts, axis=1)
    variance = sum_all(partial_sum, "factor")[None]
    deviation = jnp.sqrt(variance + epsilon)
    margin = headroom - quantile * deviation
    violation = jnp.maximum(-margin, 0.0)
    var_grad = quantile * violation / deviation
    volt_grad = (2.0 * var_grad[0][:, None, :] * factor_volts).astype(jnp.bfloat16)
    node_grads = jnp.einsum("mn,hrn->mhr", sens, volt_grad, preferred_element_type=jnp.float32)
    picked = jnp.einsum(
        "hkm,mhr->khr",
        node_hot,
        node_grads,
        precision=lax.Precision.HIGHEST,
        preferred_element_type=jnp.float32,
    )
    member_grads = (power[:, :, None] * picked).reshape(ev_count, hours * columns)
    summed = jax.ops.segment_sum(member_grads, regions, num_segments=total_regions)
    reduced = scatter_groups(summed, "feeder", _bit_groups("feeder")[::-1])
    new_loadings = loadings - step_size * reduced.reshape(reg_local, hours, columns)
    return (margin, new_loadings)


def solution(mesh):
    return jax.shard_map(
        shards,
        mesh=mesh,
        in_specs=(
            P("feeder", None, None),
            P("feeder", None, None),
            P("feeder", None, None),
            P("feeder", None, None),
            P("feeder", None),
            P("feeder", None, "factor"),
        ),
        out_specs=(P("feeder", None, None), P("feeder", None, "factor")),
        check_vma=False,
    )
```

```python
import jax
import jax.numpy as jnp
from jax import lax
from jax.sharding import PartitionSpec as P

quantile = 1.645
epsilon = 1e-06
step_size = 16.0


def _bit_count(size):
    bits = size.bit_length() - 1
    assert (1 << bits) == size
    return bits


def _exchange(x, axis, bit, size):
    perm = [(i, i ^ (1 << bit)) for i in range(size)]
    return lax.ppermute(x, axis, perm)


def gather_blocks(x, axis):
    size = lax.axis_size(axis)
    bits = _bit_count(size)
    me = lax.axis_index(axis)
    buf = x
    for step, bit in enumerate(reversed(range(bits))):
        other = _exchange(buf, axis, bit, size)
        mine = (me >> bit) & 1
        low = jnp.where(mine == 0, buf, other)
        high = jnp.where(mine == 0, other, buf)
        buf = jnp.stack([low, high], axis=step)
    return buf.reshape((size * x.shape[0],) + x.shape[1:])


def scatter_blocks(x, axis):
    size = lax.axis_size(axis)
    bits = _bit_count(size)
    me = lax.axis_index(axis)
    block = x.shape[0] // size
    buf = x.reshape((2,) * bits + (block,) + x.shape[1:])
    for bit in range(bits):
        at = bits - 1 - bit
        mine = (me >> bit) & 1
        keep = lax.dynamic_index_in_dim(buf, mine, at, keepdims=False)
        send = lax.dynamic_index_in_dim(buf, 1 - mine, at, keepdims=False)
        buf = keep + _exchange(send, axis, bit, size)
    return buf


def sum_all(x, axis):
    size = lax.axis_size(axis)
    for bit in range(_bit_count(size)):
        x = x + _exchange(x, axis, bit, size)
    return x


def _mask(j, bits):
    m = 0
    for pos, b in enumerate(bits):
        if (j >> pos) & 1:
            m |= 1 << b
    return m

def _sub(me, bits):
    s = 0
    for pos, b in enumerate(bits):
        s = s + ((me >> b) & 1) * (1 << pos)
    return s

def _send_all(x_for, axis, bits, size):
    out = {}
    for j in range(1, 1 << len(bits)):
        m = _mask(j, bits)
        out[j] = lax.ppermute(x_for(j), axis, [(i, i ^ m) for i in range(size)])
    return out

def _ordered(own, got, s, count):
    cand = jnp.stack([own] + [got[j] for j in range(1, count)])
    idx = jnp.arange(count, dtype=jnp.int32) ^ s
    return jnp.take(cand, idx, axis=0)

def gather_groups(x, axis, groups):
    size = lax.axis_size(axis)
    me = lax.axis_index(axis)
    buf = x[None]
    done = []
    for bits in groups:
        count = 1 << len(bits)
        s = _sub(me, bits)
        got = _send_all(lambda j: buf, axis, bits, size)
        stacked = _ordered(buf, got, s, count)
        buf = stacked
        done.append(bits)
    buf = buf.reshape(buf.shape[:len(groups)] + x.shape)
    order = sorted(range(len(groups)), key=lambda g: -max(groups[len(groups) - 1 - g]))
    buf = jnp.transpose(buf, order + list(range(len(groups), buf.ndim)))
    return buf.reshape((size * x.shape[0],) + x.shape[1:])

def scatter_groups(x, axis, groups):
    size = lax.axis_size(axis)
    me = lax.axis_index(axis)
    block = x.shape[0] // size
    total = sum(len(b) for b in groups)
    buf = x.reshape((2,) * total + (block,) + x.shape[1:])
    remaining = list(reversed(range(total)))
    for bits in groups:
        count = 1 << len(bits)
        s = _sub(me, bits)
        axes = [remaining.index(b) for b in reversed(bits)]
        rest = [a for a in range(len(remaining)) if a not in axes]
        buf = jnp.transpose(buf, axes + rest + list(range(len(remaining), buf.ndim)))
        buf = buf.reshape((count,) + buf.shape[len(bits):])
        remaining = [b for b in remaining if b not in bits]
        own = lax.dynamic_index_in_dim(buf, s, 0, keepdims=False)
        got = _send_all(lambda j: lax.dynamic_index_in_dim(buf, s ^ j, 0, keepdims=False), axis, bits, size)
        acc = own
        for j in range(1, count):
            acc = acc + got[j]
        buf = acc
    return buf

def sum_groups(x, axis, groups):
    size = lax.axis_size(axis)
    me = lax.axis_index(axis)
    for bits in groups:
        count = 1 << len(bits)
        s = _sub(me, bits)
        got = _send_all(lambda j: x, axis, bits, size)
        vals = _ordered(x, got, s, count)
        while vals.shape[0] > 1:
            vals = vals[0::2] + vals[1::2]
        x = vals[0]
    return x


def _bit_groups(axis):
    rest = list(range(1, _bit_count(lax.axis_size(axis))))
    pairs = [tuple(rest[max(0, i - 1) : i + 1]) for i in range(len(rest) - 1, -1, -2)]
    return pairs + [(0,)]


def _split_bf16(x):
    high = lax.reduce_precision(x, exponent_bits=8, mantissa_bits=7)
    return high.astype(jnp.bfloat16), (x - high).astype(jnp.bfloat16)


def shards(sensitivity, headroom, ev_power, ev_node, region_map, loadings):
    reg_local, hours, columns = loadings.shape
    nodes = sensitivity.shape[2]
    ev_count = ev_power.shape[2]
    total_regions = reg_local * lax.axis_size("feeder")
    packed = loadings.astype(jnp.bfloat16).reshape(reg_local, hours * columns)
    shard_rows = gather_groups(packed, "feeder", _bit_groups("feeder"))
    regions = region_map.reshape(-1)
    matches = (regions[:, None] == lax.iota(jnp.int32, total_regions)[None, :]).astype(jnp.bfloat16)
    looked = jnp.dot(matches, shard_rows, preferred_element_type=jnp.float32)
    looked = looked.reshape(ev_count, hours, columns)
    power = ev_power[0].T
    weighted = (power[:, :, None] * looked).astype(jnp.bfloat16)
    node_hot = (ev_node[0][:, :, None] == lax.iota(jnp.int32, nodes)[None, None, :]).astype(jnp.bfloat16)
    spread = jnp.einsum("khr,hkm->hrm", weighted, node_hot, preferred_element_type=jnp.float32)
    spread_hi, spread_lo = _split_bf16(spread)
    sens = sensitivity[0]
    factor_volts = jnp.einsum("hrm,mn->hrn", spread_hi, sens, preferred_element_type=jnp.float32)
    factor_volts = factor_volts + jnp.einsum("hrm,mn->hrn", spread_lo, sens, preferred_element_type=jnp.float32)
    partial_sum = jnp.sum(factor_volts * factor_volts, axis=1)
    variance = sum_all(partial_sum, "factor")[None]
    deviation = jnp.sqrt(variance + epsilon)
    margin = headroom - quantile * deviation
    violation = jnp.maximum(-margin, 0.0)
    var_grad = quantile * violation / deviation
    volt_grad = (2.0 * var_grad[0][:, None, :] * factor_volts).astype(jnp.bfloat16)
    node_grads = jnp.einsum("hrn,mn->hrm", volt_grad, sens, preferred_element_type=jnp.float32)
    both = jnp.concatenate(_split_bf16(node_grads), axis=1)
    picked_both = jnp.einsum("hkm,hrm->khr", node_hot, both, preferred_element_type=jnp.float32)
    picked = picked_both[:, :, :columns] + picked_both[:, :, columns:]
    member_grads = (power[:, :, None] * picked).reshape(ev_count, hours * columns)
    grads_hi, grads_lo = _split_bf16(member_grads)
    summed = jnp.einsum("kg,kc->gc", matches, grads_hi, preferred_element_type=jnp.float32)
    summed = summed + jnp.einsum("kg,kc->gc", matches, grads_lo, preferred_element_type=jnp.float32)
    reduced = scatter_groups(summed, "feeder", _bit_groups("feeder")[::-1])
    new_loadings = loadings - step_size * reduced.reshape(reg_local, hours, columns)
    return (margin, new_loadings)


def solution(mesh):
    return jax.shard_map(
        shards,
        mesh=mesh,
        in_specs=(
            P("feeder", None, None),
            P("feeder", None, None),
            P("feeder", None, None),
            P("feeder", None, None),
            P("feeder", None),
            P("feeder", None, "factor"),
        ),
        out_specs=(P("feeder", None, None), P("feeder", None, "factor")),
        check_vma=False,
    )
```

```python
import jax
import jax.numpy as jnp
from jax import lax
from jax.sharding import PartitionSpec as P

quantile = 1.645
epsilon = 1e-06
step_size = 16.0


def _bit_count(size):
    bits = size.bit_length() - 1
    assert (1 << bits) == size
    return bits


def _exchange(x, axis, bit, size):
    perm = [(i, i ^ (1 << bit)) for i in range(size)]
    return lax.ppermute(x, axis, perm)


def gather_blocks(x, axis):
    size = lax.axis_size(axis)
    bits = _bit_count(size)
    me = lax.axis_index(axis)
    buf = x
    for step, bit in enumerate(reversed(range(bits))):
        other = _exchange(buf, axis, bit, size)
        mine = (me >> bit) & 1
        low = jnp.where(mine == 0, buf, other)
        high = jnp.where(mine == 0, other, buf)
        buf = jnp.stack([low, high], axis=step)
    return buf.reshape((size * x.shape[0],) + x.shape[1:])


def scatter_blocks(x, axis):
    size = lax.axis_size(axis)
    bits = _bit_count(size)
    me = lax.axis_index(axis)
    block = x.shape[0] // size
    buf = x.reshape((2,) * bits + (block,) + x.shape[1:])
    for bit in range(bits):
        at = bits - 1 - bit
        mine = (me >> bit) & 1
        keep = lax.dynamic_index_in_dim(buf, mine, at, keepdims=False)
        send = lax.dynamic_index_in_dim(buf, 1 - mine, at, keepdims=False)
        buf = keep + _exchange(send, axis, bit, size)
    return buf


def sum_all(x, axis):
    size = lax.axis_size(axis)
    for bit in range(_bit_count(size)):
        x = x + _exchange(x, axis, bit, size)
    return x


def _mask(j, bits):
    m = 0
    for pos, b in enumerate(bits):
        if (j >> pos) & 1:
            m |= 1 << b
    return m

def _sub(me, bits):
    s = 0
    for pos, b in enumerate(bits):
        s = s + ((me >> b) & 1) * (1 << pos)
    return s

def _send_all(x_for, axis, bits, size):
    out = {}
    for j in range(1, 1 << len(bits)):
        m = _mask(j, bits)
        out[j] = lax.ppermute(x_for(j), axis, [(i, i ^ m) for i in range(size)])
    return out

def _ordered(own, got, s, count):
    cand = jnp.stack([own] + [got[j] for j in range(1, count)])
    idx = jnp.arange(count, dtype=jnp.int32) ^ s
    return jnp.take(cand, idx, axis=0)

def gather_groups(x, axis, groups):
    size = lax.axis_size(axis)
    me = lax.axis_index(axis)
    buf = x[None]
    done = []
    for bits in groups:
        count = 1 << len(bits)
        s = _sub(me, bits)
        got = _send_all(lambda j: buf, axis, bits, size)
        stacked = _ordered(buf, got, s, count)
        buf = stacked
        done.append(bits)
    buf = buf.reshape(buf.shape[:len(groups)] + x.shape)
    order = sorted(range(len(groups)), key=lambda g: -max(groups[len(groups) - 1 - g]))
    buf = jnp.transpose(buf, order + list(range(len(groups), buf.ndim)))
    return buf.reshape((size * x.shape[0],) + x.shape[1:])

def scatter_groups(x, axis, groups):
    size = lax.axis_size(axis)
    me = lax.axis_index(axis)
    block = x.shape[0] // size
    total = sum(len(b) for b in groups)
    buf = x.reshape((2,) * total + (block,) + x.shape[1:])
    remaining = list(reversed(range(total)))
    for bits in groups:
        count = 1 << len(bits)
        s = _sub(me, bits)
        axes = [remaining.index(b) for b in reversed(bits)]
        rest = [a for a in range(len(remaining)) if a not in axes]
        buf = jnp.transpose(buf, axes + rest + list(range(len(remaining), buf.ndim)))
        buf = buf.reshape((count,) + buf.shape[len(bits):])
        remaining = [b for b in remaining if b not in bits]
        own = lax.dynamic_index_in_dim(buf, s, 0, keepdims=False)
        got = _send_all(lambda j: lax.dynamic_index_in_dim(buf, s ^ j, 0, keepdims=False), axis, bits, size)
        acc = own
        for j in range(1, count):
            acc = acc + got[j]
        buf = acc
    return buf

def sum_groups(x, axis, groups):
    size = lax.axis_size(axis)
    me = lax.axis_index(axis)
    for bits in groups:
        count = 1 << len(bits)
        s = _sub(me, bits)
        got = _send_all(lambda j: x, axis, bits, size)
        vals = _ordered(x, got, s, count)
        while vals.shape[0] > 1:
            vals = vals[0::2] + vals[1::2]
        x = vals[0]
    return x


def _bit_groups(axis):
    rest = list(range(1, _bit_count(lax.axis_size(axis))))
    pairs = [tuple(rest[max(0, i - 1) : i + 1]) for i in range(len(rest) - 1, -1, -2)]
    return pairs + [(0,)]


def _split_bf16(x):
    high = lax.reduce_precision(x, exponent_bits=8, mantissa_bits=7)
    return high.astype(jnp.bfloat16), (x - high).astype(jnp.bfloat16)


def shards(sensitivity, headroom, ev_power, ev_node, region_map, loadings):
    reg_local, hours, columns = loadings.shape
    nodes = sensitivity.shape[2]
    ev_count = ev_power.shape[2]
    total_regions = reg_local * lax.axis_size("feeder")
    packed = loadings.astype(jnp.bfloat16).reshape(reg_local, hours * columns)
    shard_rows = gather_groups(packed, "feeder", _bit_groups("feeder"))
    regions = region_map.reshape(-1)
    matches = (regions[:, None] == lax.iota(jnp.int32, total_regions)[None, :]).astype(jnp.bfloat16)
    looked = jnp.dot(matches, shard_rows, preferred_element_type=jnp.float32)
    looked = looked.reshape(ev_count, hours, columns)
    power = ev_power[0].T
    weighted = (power[:, :, None] * looked).astype(jnp.bfloat16)
    node_hot = (ev_node[0][:, :, None] == lax.iota(jnp.int32, nodes)[None, None, :]).astype(jnp.bfloat16)
    spread = jnp.einsum("khr,hkm->hrm", weighted, node_hot, preferred_element_type=jnp.float32)
    spread_both = jnp.concatenate(_split_bf16(spread), axis=1)
    sens = sensitivity[0]
    volts_both = jnp.einsum("hrm,mn->hrn", spread_both, sens, preferred_element_type=jnp.float32)
    factor_volts = volts_both[:, :columns] + volts_both[:, columns:]
    partial_sum = jnp.sum(factor_volts * factor_volts, axis=1)
    variance = sum_all(partial_sum, "factor")[None]
    deviation = jnp.sqrt(variance + epsilon)
    margin = headroom - quantile * deviation
    violation = jnp.maximum(-margin, 0.0)
    var_grad = quantile * violation / deviation
    volt_grad = (2.0 * var_grad[0][:, None, :] * factor_volts).astype(jnp.bfloat16)
    node_grads = jnp.einsum("hrn,mn->hrm", volt_grad, sens, preferred_element_type=jnp.float32)
    both = jnp.concatenate(_split_bf16(node_grads), axis=1)
    picked_both = jnp.einsum("hkm,hrm->khr", node_hot, both, preferred_element_type=jnp.float32)
    picked = picked_both[:, :, :columns] + picked_both[:, :, columns:]
    member_grads = (power[:, :, None] * picked).reshape(ev_count, hours * columns)
    grads_hi, grads_lo = _split_bf16(member_grads)
    summed = jnp.einsum("kg,kc->gc", matches, grads_hi, preferred_element_type=jnp.float32)
    summed = summed + jnp.einsum("kg,kc->gc", matches, grads_lo, preferred_element_type=jnp.float32)
    reduced = scatter_groups(summed, "feeder", _bit_groups("feeder")[::-1])
    new_loadings = loadings - step_size * reduced.reshape(reg_local, hours, columns)
    return (margin, new_loadings)


def solution(mesh):
    return jax.shard_map(
        shards,
        mesh=mesh,
        in_specs=(
            P("feeder", None, None),
            P("feeder", None, None),
            P("feeder", None, None),
            P("feeder", None, None),
            P("feeder", None),
            P("feeder", None, "factor"),
        ),
        out_specs=(P("feeder", None, None), P("feeder", None, "factor")),
        check_vma=False,
    )
```

```python
import jax
import jax.numpy as jnp
from jax import lax
from jax.sharding import PartitionSpec as P

quantile = 1.645
epsilon = 1e-06
step_size = 16.0


def _bit_count(size):
    bits = size.bit_length() - 1
    assert (1 << bits) == size
    return bits


def _exchange(x, axis, bit, size):
    perm = [(i, i ^ (1 << bit)) for i in range(size)]
    return lax.ppermute(x, axis, perm)


def gather_blocks(x, axis):
    size = lax.axis_size(axis)
    bits = _bit_count(size)
    me = lax.axis_index(axis)
    buf = x
    for step, bit in enumerate(reversed(range(bits))):
        other = _exchange(buf, axis, bit, size)
        mine = (me >> bit) & 1
        low = jnp.where(mine == 0, buf, other)
        high = jnp.where(mine == 0, other, buf)
        buf = jnp.stack([low, high], axis=step)
    return buf.reshape((size * x.shape[0],) + x.shape[1:])


def scatter_blocks(x, axis):
    size = lax.axis_size(axis)
    bits = _bit_count(size)
    me = lax.axis_index(axis)
    block = x.shape[0] // size
    buf = x.reshape((2,) * bits + (block,) + x.shape[1:])
    for bit in range(bits):
        at = bits - 1 - bit
        mine = (me >> bit) & 1
        keep = lax.dynamic_index_in_dim(buf, mine, at, keepdims=False)
        send = lax.dynamic_index_in_dim(buf, 1 - mine, at, keepdims=False)
        buf = keep + _exchange(send, axis, bit, size)
    return buf


def sum_all(x, axis):
    size = lax.axis_size(axis)
    for bit in range(_bit_count(size)):
        x = x + _exchange(x, axis, bit, size)
    return x


def _mask(j, bits):
    m = 0
    for pos, b in enumerate(bits):
        if (j >> pos) & 1:
            m |= 1 << b
    return m

def _sub(me, bits):
    s = 0
    for pos, b in enumerate(bits):
        s = s + ((me >> b) & 1) * (1 << pos)
    return s

def _send_all(x_for, axis, bits, size):
    out = {}
    for j in range(1, 1 << len(bits)):
        m = _mask(j, bits)
        out[j] = lax.ppermute(x_for(j), axis, [(i, i ^ m) for i in range(size)])
    return out

def _ordered(own, got, s, count):
    cand = jnp.stack([own] + [got[j] for j in range(1, count)])
    idx = jnp.arange(count, dtype=jnp.int32) ^ s
    return jnp.take(cand, idx, axis=0)

def gather_groups(x, axis, groups):
    size = lax.axis_size(axis)
    me = lax.axis_index(axis)
    buf = x[None]
    done = []
    for bits in groups:
        count = 1 << len(bits)
        s = _sub(me, bits)
        got = _send_all(lambda j: buf, axis, bits, size)
        stacked = _ordered(buf, got, s, count)
        buf = stacked
        done.append(bits)
    buf = buf.reshape(buf.shape[:len(groups)] + x.shape)
    order = sorted(range(len(groups)), key=lambda g: -max(groups[len(groups) - 1 - g]))
    buf = jnp.transpose(buf, order + list(range(len(groups), buf.ndim)))
    return buf.reshape((size * x.shape[0],) + x.shape[1:])

def scatter_groups(x, axis, groups):
    size = lax.axis_size(axis)
    me = lax.axis_index(axis)
    block = x.shape[0] // size
    total = sum(len(b) for b in groups)
    buf = x.reshape((2,) * total + (block,) + x.shape[1:])
    remaining = list(reversed(range(total)))
    for bits in groups:
        count = 1 << len(bits)
        s = _sub(me, bits)
        axes = [remaining.index(b) for b in reversed(bits)]
        rest = [a for a in range(len(remaining)) if a not in axes]
        buf = jnp.transpose(buf, axes + rest + list(range(len(remaining), buf.ndim)))
        buf = buf.reshape((count,) + buf.shape[len(bits):])
        remaining = [b for b in remaining if b not in bits]
        own = lax.dynamic_index_in_dim(buf, s, 0, keepdims=False)
        got = _send_all(lambda j: lax.dynamic_index_in_dim(buf, s ^ j, 0, keepdims=False), axis, bits, size)
        acc = own
        for j in range(1, count):
            acc = acc + got[j]
        buf = acc
    return buf

def sum_groups(x, axis, groups):
    size = lax.axis_size(axis)
    me = lax.axis_index(axis)
    for bits in groups:
        count = 1 << len(bits)
        s = _sub(me, bits)
        got = _send_all(lambda j: x, axis, bits, size)
        vals = _ordered(x, got, s, count)
        while vals.shape[0] > 1:
            vals = vals[0::2] + vals[1::2]
        x = vals[0]
    return x


CHUNKS = 2


def _bit_groups(axis):
    rest = list(range(1, _bit_count(lax.axis_size(axis))))
    pairs = [tuple(rest[max(0, i - 1) : i + 1]) for i in range(len(rest) - 1, -1, -2)]
    return pairs + [(0,)]


def _split_bf16(x):
    high = lax.reduce_precision(x, exponent_bits=8, mantissa_bits=7)
    return high.astype(jnp.bfloat16), (x - high).astype(jnp.bfloat16)


def shards(sensitivity, headroom, ev_power, ev_node, region_map, loadings):
    reg_local, hours, columns = loadings.shape
    nodes = sensitivity.shape[2]
    ev_count = ev_power.shape[2]
    total_regions = reg_local * lax.axis_size("feeder")
    packed = loadings.astype(jnp.bfloat16).reshape(reg_local, hours * columns)
    shard_rows = gather_groups(packed, "feeder", _bit_groups("feeder"))
    regions = region_map.reshape(-1)
    matches = (regions[:, None] == lax.iota(jnp.int32, total_regions)[None, :]).astype(jnp.bfloat16)
    looked = jnp.dot(matches, shard_rows, preferred_element_type=jnp.float32)
    looked = looked.reshape(ev_count, hours, columns)
    power = ev_power[0].T
    weighted = (power[:, :, None] * looked).astype(jnp.bfloat16)
    node_hot = (ev_node[0][:, :, None] == lax.iota(jnp.int32, nodes)[None, None, :]).astype(jnp.bfloat16)
    sens = sensitivity[0]
    span = hours // CHUNKS
    volts_parts = []
    variance_parts = []
    for chunk in range(CHUNKS):
        at = slice(chunk * span, (chunk + 1) * span)
        spread = jnp.einsum("khr,hkm->hrm", weighted[:, at], node_hot[at], preferred_element_type=jnp.float32)
        spread_both = jnp.concatenate(_split_bf16(spread), axis=1)
        volts_both = jnp.einsum("hrm,mn->hrn", spread_both, sens, preferred_element_type=jnp.float32)
        part = volts_both[:, :columns] + volts_both[:, columns:]
        volts_parts.append(part)
        variance_parts.append(sum_all(jnp.sum(part * part, axis=1), "factor"))
    factor_volts = jnp.concatenate(volts_parts, axis=0)
    variance = jnp.concatenate(variance_parts, axis=0)[None]
    deviation = jnp.sqrt(variance + epsilon)
    margin = headroom - quantile * deviation
    violation = jnp.maximum(-margin, 0.0)
    var_grad = quantile * violation / deviation
    volt_grad = (2.0 * var_grad[0][:, None, :] * factor_volts).astype(jnp.bfloat16)
    node_grads = jnp.einsum("hrn,mn->hrm", volt_grad, sens, preferred_element_type=jnp.float32)
    both = jnp.concatenate(_split_bf16(node_grads), axis=1)
    picked_both = jnp.einsum("hkm,hrm->khr", node_hot, both, preferred_element_type=jnp.float32)
    picked = picked_both[:, :, :columns] + picked_both[:, :, columns:]
    member_grads = (power[:, :, None] * picked).reshape(ev_count, hours * columns)
    grads_hi, grads_lo = _split_bf16(member_grads)
    summed = jnp.einsum("kg,kc->gc", matches, grads_hi, preferred_element_type=jnp.float32)
    summed = summed + jnp.einsum("kg,kc->gc", matches, grads_lo, preferred_element_type=jnp.float32)
    reduced = scatter_groups(summed, "feeder", _bit_groups("feeder")[::-1])
    new_loadings = loadings - step_size * reduced.reshape(reg_local, hours, columns)
    return (margin, new_loadings)


def solution(mesh):
    return jax.shard_map(
        shards,
        mesh=mesh,
        in_specs=(
            P("feeder", None, None),
            P("feeder", None, None),
            P("feeder", None, None),
            P("feeder", None, None),
            P("feeder", None),
            P("feeder", None, "factor"),
        ),
        out_specs=(P("feeder", None, None), P("feeder", None, "factor")),
        check_vma=False,
    )
```

```python
import jax
import jax.numpy as jnp
from jax import lax
from jax.sharding import PartitionSpec as P

quantile = 1.645
epsilon = 1e-06
step_size = 16.0


def _bit_count(size):
    bits = size.bit_length() - 1
    assert (1 << bits) == size
    return bits


def _exchange(x, axis, bit, size):
    perm = [(i, i ^ (1 << bit)) for i in range(size)]
    return lax.ppermute(x, axis, perm)


def gather_blocks(x, axis):
    size = lax.axis_size(axis)
    bits = _bit_count(size)
    me = lax.axis_index(axis)
    buf = x
    for step, bit in enumerate(reversed(range(bits))):
        other = _exchange(buf, axis, bit, size)
        mine = (me >> bit) & 1
        low = jnp.where(mine == 0, buf, other)
        high = jnp.where(mine == 0, other, buf)
        buf = jnp.stack([low, high], axis=step)
    return buf.reshape((size * x.shape[0],) + x.shape[1:])


def scatter_blocks(x, axis):
    size = lax.axis_size(axis)
    bits = _bit_count(size)
    me = lax.axis_index(axis)
    block = x.shape[0] // size
    buf = x.reshape((2,) * bits + (block,) + x.shape[1:])
    for bit in range(bits):
        at = bits - 1 - bit
        mine = (me >> bit) & 1
        keep = lax.dynamic_index_in_dim(buf, mine, at, keepdims=False)
        send = lax.dynamic_index_in_dim(buf, 1 - mine, at, keepdims=False)
        buf = keep + _exchange(send, axis, bit, size)
    return buf


def sum_all(x, axis):
    size = lax.axis_size(axis)
    for bit in range(_bit_count(size)):
        x = x + _exchange(x, axis, bit, size)
    return x


def _mask(j, bits):
    m = 0
    for pos, b in enumerate(bits):
        if (j >> pos) & 1:
            m |= 1 << b
    return m

def _sub(me, bits):
    s = 0
    for pos, b in enumerate(bits):
        s = s + ((me >> b) & 1) * (1 << pos)
    return s

def _send_all(x_for, axis, bits, size):
    out = {}
    for j in range(1, 1 << len(bits)):
        m = _mask(j, bits)
        out[j] = lax.ppermute(x_for(j), axis, [(i, i ^ m) for i in range(size)])
    return out

def _ordered(own, got, s, count):
    cand = jnp.stack([own] + [got[j] for j in range(1, count)])
    idx = jnp.arange(count, dtype=jnp.int32) ^ s
    return jnp.take(cand, idx, axis=0)

def gather_groups(x, axis, groups):
    size = lax.axis_size(axis)
    me = lax.axis_index(axis)
    buf = x[None]
    done = []
    for bits in groups:
        count = 1 << len(bits)
        s = _sub(me, bits)
        got = _send_all(lambda j: buf, axis, bits, size)
        stacked = _ordered(buf, got, s, count)
        buf = stacked
        done.append(bits)
    buf = buf.reshape(buf.shape[:len(groups)] + x.shape)
    order = sorted(range(len(groups)), key=lambda g: -max(groups[len(groups) - 1 - g]))
    buf = jnp.transpose(buf, order + list(range(len(groups), buf.ndim)))
    return buf.reshape((size * x.shape[0],) + x.shape[1:])

def scatter_groups(x, axis, groups):
    size = lax.axis_size(axis)
    me = lax.axis_index(axis)
    block = x.shape[0] // size
    total = sum(len(b) for b in groups)
    buf = x.reshape((2,) * total + (block,) + x.shape[1:])
    remaining = list(reversed(range(total)))
    for bits in groups:
        count = 1 << len(bits)
        s = _sub(me, bits)
        axes = [remaining.index(b) for b in reversed(bits)]
        rest = [a for a in range(len(remaining)) if a not in axes]
        buf = jnp.transpose(buf, axes + rest + list(range(len(remaining), buf.ndim)))
        buf = buf.reshape((count,) + buf.shape[len(bits):])
        remaining = [b for b in remaining if b not in bits]
        own = lax.dynamic_index_in_dim(buf, s, 0, keepdims=False)
        got = _send_all(lambda j: lax.dynamic_index_in_dim(buf, s ^ j, 0, keepdims=False), axis, bits, size)
        acc = own
        for j in range(1, count):
            acc = acc + got[j]
        buf = acc
    return buf

def sum_groups(x, axis, groups):
    size = lax.axis_size(axis)
    me = lax.axis_index(axis)
    for bits in groups:
        count = 1 << len(bits)
        s = _sub(me, bits)
        got = _send_all(lambda j: x, axis, bits, size)
        vals = _ordered(x, got, s, count)
        while vals.shape[0] > 1:
            vals = vals[0::2] + vals[1::2]
        x = vals[0]
    return x


CHUNKS = 2


def _bit_groups(axis):
    rest = list(range(1, _bit_count(lax.axis_size(axis))))
    pairs = [tuple(rest[max(0, i - 1) : i + 1]) for i in range(len(rest) - 1, -1, -2)]
    return pairs + [(0,)]


def _split_bf16(x):
    high = lax.reduce_precision(x, exponent_bits=8, mantissa_bits=7)
    return high.astype(jnp.bfloat16), (x - high).astype(jnp.bfloat16)


def shards(sensitivity, headroom, ev_power, ev_node, region_map, loadings):
    reg_local, hours, columns = loadings.shape
    nodes = sensitivity.shape[2]
    ev_count = ev_power.shape[2]
    total_regions = reg_local * lax.axis_size("feeder")
    packed = loadings.astype(jnp.bfloat16).reshape(reg_local, hours * columns)
    shard_rows = gather_groups(packed, "feeder", _bit_groups("feeder"))
    regions = region_map.reshape(-1)
    matches = (regions[:, None] == lax.iota(jnp.int32, total_regions)[None, :]).astype(jnp.bfloat16)
    looked = jnp.dot(matches, shard_rows, preferred_element_type=jnp.float32)
    looked = looked.reshape(ev_count, hours, columns)
    power = ev_power[0].T
    weighted = (power[:, :, None] * looked).astype(jnp.bfloat16)
    node_hot = (ev_node[0][:, :, None] == lax.iota(jnp.int32, nodes)[None, None, :]).astype(jnp.bfloat16)
    sens = sensitivity[0]
    span = hours // CHUNKS
    row_parts = []
    volts_parts = []
    variance_parts = []
    for chunk in range(CHUNKS):
        at = slice(chunk * span, (chunk + 1) * span)
        rows = jnp.einsum("hkm,mn->hkn", node_hot[at], sens, preferred_element_type=jnp.float32)
        rows = rows.astype(jnp.bfloat16)
        part = jnp.einsum("khr,hkn->hrn", weighted[:, at], rows, preferred_element_type=jnp.float32)
        row_parts.append(rows)
        volts_parts.append(part)
        variance_parts.append(sum_all(jnp.sum(part * part, axis=1), "factor"))
    factor_volts = jnp.concatenate(volts_parts, axis=0)
    sens_rows = jnp.concatenate(row_parts, axis=0)
    variance = jnp.concatenate(variance_parts, axis=0)[None]
    deviation = jnp.sqrt(variance + epsilon)
    margin = headroom - quantile * deviation
    violation = jnp.maximum(-margin, 0.0)
    var_grad = quantile * violation / deviation
    volt_grad = (2.0 * var_grad[0][:, None, :] * factor_volts).astype(jnp.bfloat16)
    picked = jnp.einsum("hkn,hrn->khr", sens_rows, volt_grad, preferred_element_type=jnp.float32)
    member_grads = (power[:, :, None] * picked).reshape(ev_count, hours * columns)
    grads_hi, grads_lo = _split_bf16(member_grads)
    summed = jnp.einsum("kg,kc->gc", matches, grads_hi, preferred_element_type=jnp.float32)
    summed = summed + jnp.einsum("kg,kc->gc", matches, grads_lo, preferred_element_type=jnp.float32)
    reduced = scatter_groups(summed, "feeder", _bit_groups("feeder")[::-1])
    new_loadings = loadings - step_size * reduced.reshape(reg_local, hours, columns)
    return (margin, new_loadings)


def solution(mesh):
    return jax.shard_map(
        shards,
        mesh=mesh,
        in_specs=(
            P("feeder", None, None),
            P("feeder", None, None),
            P("feeder", None, None),
            P("feeder", None, None),
            P("feeder", None),
            P("feeder", None, "factor"),
        ),
        out_specs=(P("feeder", None, None), P("feeder", None, "factor")),
        check_vma=False,
    )
```

```python
import jax
import jax.numpy as jnp
from jax import lax
from jax.sharding import PartitionSpec as P

quantile = 1.645
epsilon = 1e-06
step_size = 16.0


def _bit_count(size):
    bits = size.bit_length() - 1
    assert (1 << bits) == size
    return bits


def _exchange(x, axis, bit, size):
    perm = [(i, i ^ (1 << bit)) for i in range(size)]
    return lax.ppermute(x, axis, perm)


def gather_blocks(x, axis):
    size = lax.axis_size(axis)
    bits = _bit_count(size)
    me = lax.axis_index(axis)
    buf = x
    for step, bit in enumerate(reversed(range(bits))):
        other = _exchange(buf, axis, bit, size)
        mine = (me >> bit) & 1
        low = jnp.where(mine == 0, buf, other)
        high = jnp.where(mine == 0, other, buf)
        buf = jnp.stack([low, high], axis=step)
    return buf.reshape((size * x.shape[0],) + x.shape[1:])


def scatter_blocks(x, axis):
    size = lax.axis_size(axis)
    bits = _bit_count(size)
    me = lax.axis_index(axis)
    block = x.shape[0] // size
    buf = x.reshape((2,) * bits + (block,) + x.shape[1:])
    for bit in range(bits):
        at = bits - 1 - bit
        mine = (me >> bit) & 1
        keep = lax.dynamic_index_in_dim(buf, mine, at, keepdims=False)
        send = lax.dynamic_index_in_dim(buf, 1 - mine, at, keepdims=False)
        buf = keep + _exchange(send, axis, bit, size)
    return buf


def sum_all(x, axis):
    size = lax.axis_size(axis)
    for bit in range(_bit_count(size)):
        x = x + _exchange(x, axis, bit, size)
    return x


def _mask(j, bits):
    m = 0
    for pos, b in enumerate(bits):
        if (j >> pos) & 1:
            m |= 1 << b
    return m

def _sub(me, bits):
    s = 0
    for pos, b in enumerate(bits):
        s = s + ((me >> b) & 1) * (1 << pos)
    return s

def _send_all(x_for, axis, bits, size):
    out = {}
    for j in range(1, 1 << len(bits)):
        m = _mask(j, bits)
        out[j] = lax.ppermute(x_for(j), axis, [(i, i ^ m) for i in range(size)])
    return out

def _ordered(own, got, s, count):
    cand = jnp.stack([own] + [got[j] for j in range(1, count)])
    idx = jnp.arange(count, dtype=jnp.int32) ^ s
    return jnp.take(cand, idx, axis=0)

def gather_groups(x, axis, groups, hooks=()):
    size = lax.axis_size(axis)
    me = lax.axis_index(axis)
    buf = x[None]
    done = []
    for bits in groups:
        count = 1 << len(bits)
        s = _sub(me, bits)
        got = _send_all(lambda j: buf, axis, bits, size)
        stacked = _ordered(buf, got, s, count)
        buf = stacked
        if len(done) < len(hooks):
            buf = hooks[len(done)](buf)
        done.append(bits)
    buf = buf.reshape(buf.shape[:len(groups)] + x.shape)
    order = sorted(range(len(groups)), key=lambda g: -max(groups[len(groups) - 1 - g]))
    buf = jnp.transpose(buf, order + list(range(len(groups), buf.ndim)))
    return buf.reshape((size * x.shape[0],) + x.shape[1:])

def scatter_groups(x, axis, groups):
    size = lax.axis_size(axis)
    me = lax.axis_index(axis)
    block = x.shape[0] // size
    total = sum(len(b) for b in groups)
    buf = x.reshape((2,) * total + (block,) + x.shape[1:])
    remaining = list(reversed(range(total)))
    for bits in groups:
        count = 1 << len(bits)
        s = _sub(me, bits)
        axes = [remaining.index(b) for b in reversed(bits)]
        rest = [a for a in range(len(remaining)) if a not in axes]
        buf = jnp.transpose(buf, axes + rest + list(range(len(remaining), buf.ndim)))
        buf = buf.reshape((count,) + buf.shape[len(bits):])
        remaining = [b for b in remaining if b not in bits]
        own = lax.dynamic_index_in_dim(buf, s, 0, keepdims=False)
        got = _send_all(lambda j: lax.dynamic_index_in_dim(buf, s ^ j, 0, keepdims=False), axis, bits, size)
        acc = own
        for j in range(1, count):
            acc = acc + got[j]
        buf = acc
    return buf

def sum_groups(x, axis, groups):
    size = lax.axis_size(axis)
    me = lax.axis_index(axis)
    for bits in groups:
        count = 1 << len(bits)
        s = _sub(me, bits)
        got = _send_all(lambda j: x, axis, bits, size)
        vals = _ordered(x, got, s, count)
        while vals.shape[0] > 1:
            vals = vals[0::2] + vals[1::2]
        x = vals[0]
    return x


CHUNKS = 2


def _bit_groups(axis):
    rest = list(range(1, _bit_count(lax.axis_size(axis))))
    pairs = [tuple(rest[max(0, i - 1) : i + 1]) for i in range(len(rest) - 1, -1, -2)]
    return pairs + [(0,)]


def _split_bf16(x):
    high = lax.reduce_precision(x, exponent_bits=8, mantissa_bits=7)
    return high.astype(jnp.bfloat16), (x - high).astype(jnp.bfloat16)


def shards(sensitivity, headroom, ev_power, ev_node, region_map, loadings):
    reg_local, hours, columns = loadings.shape
    nodes = sensitivity.shape[2]
    ev_count = ev_power.shape[2]
    total_regions = reg_local * lax.axis_size("feeder")
    packed = loadings.astype(jnp.bfloat16).reshape(reg_local, hours * columns)
    node_hot = (ev_node[0][:, :, None] == lax.iota(jnp.int32, nodes)[None, None, :]).astype(jnp.bfloat16)
    span = hours // CHUNKS
    hot_parts = [node_hot[chunk * span : (chunk + 1) * span] for chunk in range(CHUNKS)]
    sens = sensitivity[0]

    def rows_of(hot):
        rows = jnp.einsum("hkm,mn->hkn", hot, sens, preferred_element_type=jnp.float32)
        return rows.astype(jnp.bfloat16)

    later = {}

    def after_first(buf):
        buf, hot = lax.optimization_barrier((buf, hot_parts[1]))
        later["rows"] = rows_of(hot)
        return buf

    def after_second(buf):
        buf, later["rows"] = lax.optimization_barrier((buf, later["rows"]))
        return buf

    hooks = (after_first, after_second) if CHUNKS == 2 else ()
    shard_rows = gather_groups(packed, "feeder", _bit_groups("feeder"), hooks)
    row_list = [rows_of(hot_parts[0]), later["rows"]] if CHUNKS == 2 else [rows_of(h) for h in hot_parts]
    regions = region_map.reshape(-1)
    matches = (regions[:, None] == lax.iota(jnp.int32, total_regions)[None, :]).astype(jnp.bfloat16)
    looked = jnp.dot(matches, shard_rows, preferred_element_type=jnp.float32)
    looked = looked.reshape(ev_count, hours, columns)
    power = ev_power[0].T
    weighted = (power[:, :, None] * looked).astype(jnp.bfloat16)
    row_parts = []
    volts_parts = []
    variance_parts = []
    for chunk in range(CHUNKS):
        at = slice(chunk * span, (chunk + 1) * span)
        rows = row_list[chunk]
        part = jnp.einsum("khr,hkn->hrn", weighted[:, at], rows, preferred_element_type=jnp.float32)
        row_parts.append(rows)
        volts_parts.append(part)
        variance_parts.append(sum_all(jnp.sum(part * part, axis=1), "factor"))
    factor_volts = jnp.concatenate(volts_parts, axis=0)
    sens_rows = jnp.concatenate(row_parts, axis=0)
    variance = jnp.concatenate(variance_parts, axis=0)[None]
    deviation = jnp.sqrt(variance + epsilon)
    margin = headroom - quantile * deviation
    violation = jnp.maximum(-margin, 0.0)
    var_grad = quantile * violation / deviation
    volt_grad = (2.0 * var_grad[0][:, None, :] * factor_volts).astype(jnp.bfloat16)
    picked = jnp.einsum("hkn,hrn->khr", sens_rows, volt_grad, preferred_element_type=jnp.float32)
    member_grads = (power[:, :, None] * picked).reshape(ev_count, hours * columns)
    grads_hi, grads_lo = _split_bf16(member_grads)
    summed = jnp.einsum("kg,kc->gc", matches, grads_hi, preferred_element_type=jnp.float32)
    summed = summed + jnp.einsum("kg,kc->gc", matches, grads_lo, preferred_element_type=jnp.float32)
    reduced = scatter_groups(summed, "feeder", _bit_groups("feeder")[::-1])
    new_loadings = loadings - step_size * reduced.reshape(reg_local, hours, columns)
    return (margin, new_loadings)


def solution(mesh):
    return jax.shard_map(
        shards,
        mesh=mesh,
        in_specs=(
            P("feeder", None, None),
            P("feeder", None, None),
            P("feeder", None, None),
            P("feeder", None, None),
            P("feeder", None),
            P("feeder", None, "factor"),
        ),
        out_specs=(P("feeder", None, None), P("feeder", None, "factor")),
        check_vma=False,
    )
```

```python
import jax
import jax.numpy as jnp
from jax import lax
from jax.sharding import PartitionSpec as P

quantile = 1.645
epsilon = 1e-06
step_size = 16.0


def _bit_count(size):
    bits = size.bit_length() - 1
    assert (1 << bits) == size
    return bits


def _exchange(x, axis, bit, size):
    perm = [(i, i ^ (1 << bit)) for i in range(size)]
    return lax.ppermute(x, axis, perm)


def gather_blocks(x, axis):
    size = lax.axis_size(axis)
    bits = _bit_count(size)
    me = lax.axis_index(axis)
    buf = x
    for step, bit in enumerate(reversed(range(bits))):
        other = _exchange(buf, axis, bit, size)
        mine = (me >> bit) & 1
        low = jnp.where(mine == 0, buf, other)
        high = jnp.where(mine == 0, other, buf)
        buf = jnp.stack([low, high], axis=step)
    return buf.reshape((size * x.shape[0],) + x.shape[1:])


def scatter_blocks(x, axis):
    size = lax.axis_size(axis)
    bits = _bit_count(size)
    me = lax.axis_index(axis)
    block = x.shape[0] // size
    buf = x.reshape((2,) * bits + (block,) + x.shape[1:])
    for bit in range(bits):
        at = bits - 1 - bit
        mine = (me >> bit) & 1
        keep = lax.dynamic_index_in_dim(buf, mine, at, keepdims=False)
        send = lax.dynamic_index_in_dim(buf, 1 - mine, at, keepdims=False)
        buf = keep + _exchange(send, axis, bit, size)
    return buf


def sum_all(x, axis):
    size = lax.axis_size(axis)
    for bit in range(_bit_count(size)):
        x = x + _exchange(x, axis, bit, size)
    return x


def _mask(j, bits):
    m = 0
    for pos, b in enumerate(bits):
        if (j >> pos) & 1:
            m |= 1 << b
    return m

def _sub(me, bits):
    s = 0
    for pos, b in enumerate(bits):
        s = s + ((me >> b) & 1) * (1 << pos)
    return s

def _send_all(x_for, axis, bits, size):
    out = {}
    for j in range(1, 1 << len(bits)):
        m = _mask(j, bits)
        out[j] = lax.ppermute(x_for(j), axis, [(i, i ^ m) for i in range(size)])
    return out

def _ordered(own, got, s, count):
    cand = jnp.stack([own] + [got[j] for j in range(1, count)])
    idx = jnp.arange(count, dtype=jnp.int32) ^ s
    return jnp.take(cand, idx, axis=0)

def gather_groups(x, axis, groups):
    size = lax.axis_size(axis)
    me = lax.axis_index(axis)
    buf = x[None]
    done = []
    for bits in groups:
        count = 1 << len(bits)
        s = _sub(me, bits)
        got = _send_all(lambda j: buf, axis, bits, size)
        stacked = _ordered(buf, got, s, count)
        buf = stacked
        done.append(bits)
    buf = buf.reshape(buf.shape[:len(groups)] + x.shape)
    order = sorted(range(len(groups)), key=lambda g: -max(groups[len(groups) - 1 - g]))
    buf = jnp.transpose(buf, order + list(range(len(groups), buf.ndim)))
    return buf.reshape((size * x.shape[0],) + x.shape[1:])

def scatter_groups(x, axis, groups):
    size = lax.axis_size(axis)
    me = lax.axis_index(axis)
    block = x.shape[0] // size
    total = sum(len(b) for b in groups)
    buf = x.reshape((2,) * total + (block,) + x.shape[1:])
    remaining = list(reversed(range(total)))
    for bits in groups:
        count = 1 << len(bits)
        s = _sub(me, bits)
        axes = [remaining.index(b) for b in reversed(bits)]
        rest = [a for a in range(len(remaining)) if a not in axes]
        buf = jnp.transpose(buf, axes + rest + list(range(len(remaining), buf.ndim)))
        buf = buf.reshape((count,) + buf.shape[len(bits):])
        remaining = [b for b in remaining if b not in bits]
        own = lax.dynamic_index_in_dim(buf, s, 0, keepdims=False)
        got = _send_all(lambda j: lax.dynamic_index_in_dim(buf, s ^ j, 0, keepdims=False), axis, bits, size)
        acc = own
        for j in range(1, count):
            acc = acc + got[j]
        buf = acc
    return buf

def sum_groups(x, axis, groups):
    size = lax.axis_size(axis)
    me = lax.axis_index(axis)
    for bits in groups:
        count = 1 << len(bits)
        s = _sub(me, bits)
        got = _send_all(lambda j: x, axis, bits, size)
        vals = _ordered(x, got, s, count)
        while vals.shape[0] > 1:
            vals = vals[0::2] + vals[1::2]
        x = vals[0]
    return x


CHUNKS = 2


def _bit_groups(axis):
    rest = list(range(1, _bit_count(lax.axis_size(axis))))
    pairs = [tuple(rest[max(0, i - 1) : i + 1]) for i in range(len(rest) - 1, -1, -2)]
    return pairs + [(0,)]


def _split_bf16(x):
    high = lax.reduce_precision(x, exponent_bits=8, mantissa_bits=7)
    return high.astype(jnp.bfloat16), (x - high).astype(jnp.bfloat16)


def shards(sensitivity, headroom, ev_power, ev_node, region_map, loadings):
    reg_local, hours, columns = loadings.shape
    nodes = sensitivity.shape[2]
    ev_count = ev_power.shape[2]
    total_regions = reg_local * lax.axis_size("feeder")
    packed = loadings.astype(jnp.bfloat16).reshape(reg_local, hours * columns)
    shard_rows = gather_groups(packed, "feeder", _bit_groups("feeder"))
    regions = region_map.reshape(-1)
    matches = (regions[:, None] == lax.iota(jnp.int32, total_regions)[None, :]).astype(jnp.bfloat16)
    looked = jnp.dot(matches, shard_rows, preferred_element_type=jnp.float32)
    looked = looked.reshape(ev_count, hours, columns)
    power = ev_power[0].T
    weighted = (power[:, :, None] * looked).astype(jnp.bfloat16)
    node_hot = (ev_node[0][:, :, None] == lax.iota(jnp.int32, nodes)[None, None, :]).astype(jnp.bfloat16)
    sens = sensitivity[0]
    span = hours // 2
    early, late = slice(0, span), slice(span, hours)
    rows = jnp.einsum("hkm,mn->hkn", node_hot[early], sens, preferred_element_type=jnp.float32)
    rows = rows.astype(jnp.bfloat16)
    volts_early = jnp.einsum("khr,hkn->hrn", weighted[:, early], rows, preferred_element_type=jnp.float32)
    variance_early = sum_all(jnp.sum(volts_early * volts_early, axis=1), "factor")
    spread = jnp.einsum("khr,hkm->hrm", weighted[:, late], node_hot[late], preferred_element_type=jnp.float32)
    spread_both = jnp.concatenate(_split_bf16(spread), axis=1)
    volts_both = jnp.einsum("hrm,mn->hrn", spread_both, sens, preferred_element_type=jnp.float32)
    volts_late = volts_both[:, :columns] + volts_both[:, columns:]
    variance_late = sum_all(jnp.sum(volts_late * volts_late, axis=1), "factor")
    factor_volts = jnp.concatenate([volts_early, volts_late], axis=0)
    variance = jnp.concatenate([variance_early, variance_late], axis=0)[None]
    deviation = jnp.sqrt(variance + epsilon)
    margin = headroom - quantile * deviation
    violation = jnp.maximum(-margin, 0.0)
    var_grad = quantile * violation / deviation
    volt_grad = (2.0 * var_grad[0][:, None, :] * factor_volts).astype(jnp.bfloat16)
    picked_early = jnp.einsum("hkn,hrn->khr", rows, volt_grad[early], preferred_element_type=jnp.float32)
    node_grads = jnp.einsum("hrn,mn->hrm", volt_grad[late], sens, preferred_element_type=jnp.float32)
    both = jnp.concatenate(_split_bf16(node_grads), axis=1)
    picked_both = jnp.einsum("hkm,hrm->khr", node_hot[late], both, preferred_element_type=jnp.float32)
    picked_late = picked_both[:, :, :columns] + picked_both[:, :, columns:]
    picked = jnp.concatenate([picked_early, picked_late], axis=1)
    member_grads = (power[:, :, None] * picked).reshape(ev_count, hours * columns)
    grads_hi, grads_lo = _split_bf16(member_grads)
    summed = jnp.einsum("kg,kc->gc", matches, grads_hi, preferred_element_type=jnp.float32)
    summed = summed + jnp.einsum("kg,kc->gc", matches, grads_lo, preferred_element_type=jnp.float32)
    reduced = scatter_groups(summed, "feeder", _bit_groups("feeder")[::-1])
    new_loadings = loadings - step_size * reduced.reshape(reg_local, hours, columns)
    return (margin, new_loadings)


def solution(mesh):
    return jax.shard_map(
        shards,
        mesh=mesh,
        in_specs=(
            P("feeder", None, None),
            P("feeder", None, None),
            P("feeder", None, None),
            P("feeder", None, None),
            P("feeder", None),
            P("feeder", None, "factor"),
        ),
        out_specs=(P("feeder", None, None), P("feeder", None, "factor")),
        check_vma=False,
    )
```

```python
import jax
import jax.numpy as jnp
from jax import lax
from jax.sharding import PartitionSpec as P

quantile = 1.645
epsilon = 1e-06
step_size = 16.0


def _bit_count(size):
    bits = size.bit_length() - 1
    assert (1 << bits) == size
    return bits


def _exchange(x, axis, bit, size):
    perm = [(i, i ^ (1 << bit)) for i in range(size)]
    return lax.ppermute(x, axis, perm)


def gather_blocks(x, axis):
    size = lax.axis_size(axis)
    bits = _bit_count(size)
    me = lax.axis_index(axis)
    buf = x
    for step, bit in enumerate(reversed(range(bits))):
        other = _exchange(buf, axis, bit, size)
        mine = (me >> bit) & 1
        low = jnp.where(mine == 0, buf, other)
        high = jnp.where(mine == 0, other, buf)
        buf = jnp.stack([low, high], axis=step)
    return buf.reshape((size * x.shape[0],) + x.shape[1:])


def scatter_blocks(x, axis):
    size = lax.axis_size(axis)
    bits = _bit_count(size)
    me = lax.axis_index(axis)
    block = x.shape[0] // size
    buf = x.reshape((2,) * bits + (block,) + x.shape[1:])
    for bit in range(bits):
        at = bits - 1 - bit
        mine = (me >> bit) & 1
        keep = lax.dynamic_index_in_dim(buf, mine, at, keepdims=False)
        send = lax.dynamic_index_in_dim(buf, 1 - mine, at, keepdims=False)
        buf = keep + _exchange(send, axis, bit, size)
    return buf


def sum_all(x, axis):
    size = lax.axis_size(axis)
    for bit in range(_bit_count(size)):
        x = x + _exchange(x, axis, bit, size)
    return x


def _mask(j, bits):
    m = 0
    for pos, b in enumerate(bits):
        if (j >> pos) & 1:
            m |= 1 << b
    return m

def _sub(me, bits):
    s = 0
    for pos, b in enumerate(bits):
        s = s + ((me >> b) & 1) * (1 << pos)
    return s

def _send_all(x_for, axis, bits, size):
    out = {}
    for j in range(1, 1 << len(bits)):
        m = _mask(j, bits)
        out[j] = lax.ppermute(x_for(j), axis, [(i, i ^ m) for i in range(size)])
    return out

def _ordered(own, got, s, count):
    cand = jnp.stack([own] + [got[j] for j in range(1, count)])
    idx = jnp.arange(count, dtype=jnp.int32) ^ s
    return jnp.take(cand, idx, axis=0)

def gather_groups(x, axis, groups):
    size = lax.axis_size(axis)
    me = lax.axis_index(axis)
    buf = x[None]
    done = []
    for bits in groups:
        count = 1 << len(bits)
        s = _sub(me, bits)
        got = _send_all(lambda j: buf, axis, bits, size)
        stacked = _ordered(buf, got, s, count)
        buf = stacked
        done.append(bits)
    buf = buf.reshape(buf.shape[:len(groups)] + x.shape)
    order = sorted(range(len(groups)), key=lambda g: -max(groups[len(groups) - 1 - g]))
    buf = jnp.transpose(buf, order + list(range(len(groups), buf.ndim)))
    return buf.reshape((size * x.shape[0],) + x.shape[1:])

def scatter_groups(x, axis, groups):
    size = lax.axis_size(axis)
    me = lax.axis_index(axis)
    block = x.shape[0] // size
    total = sum(len(b) for b in groups)
    buf = x.reshape((2,) * total + (block,) + x.shape[1:])
    remaining = list(reversed(range(total)))
    for bits in groups:
        count = 1 << len(bits)
        s = _sub(me, bits)
        axes = [remaining.index(b) for b in reversed(bits)]
        rest = [a for a in range(len(remaining)) if a not in axes]
        buf = jnp.transpose(buf, axes + rest + list(range(len(remaining), buf.ndim)))
        buf = buf.reshape((count,) + buf.shape[len(bits):])
        remaining = [b for b in remaining if b not in bits]
        own = lax.dynamic_index_in_dim(buf, s, 0, keepdims=False)
        got = _send_all(lambda j: lax.dynamic_index_in_dim(buf, s ^ j, 0, keepdims=False), axis, bits, size)
        acc = own
        for j in range(1, count):
            acc = acc + got[j]
        buf = acc
    return buf

def sum_groups(x, axis, groups):
    size = lax.axis_size(axis)
    me = lax.axis_index(axis)
    for bits in groups:
        count = 1 << len(bits)
        s = _sub(me, bits)
        got = _send_all(lambda j: x, axis, bits, size)
        vals = _ordered(x, got, s, count)
        while vals.shape[0] > 1:
            vals = vals[0::2] + vals[1::2]
        x = vals[0]
    return x


CHUNKS = 2


def _bit_groups(axis):
    rest = list(range(1, _bit_count(lax.axis_size(axis))))
    pairs = [tuple(rest[max(0, i - 1) : i + 1]) for i in range(len(rest) - 1, -1, -2)]
    return pairs + [(0,)]


def _split_bf16(x):
    high = lax.reduce_precision(x, exponent_bits=8, mantissa_bits=7)
    return high.astype(jnp.bfloat16), (x - high).astype(jnp.bfloat16)


def shards(sensitivity, headroom, ev_power, ev_node, region_map, loadings):
    reg_local, hours, columns = loadings.shape
    nodes = sensitivity.shape[2]
    ev_count = ev_power.shape[2]
    total_regions = reg_local * lax.axis_size("feeder")
    packed = loadings.astype(jnp.bfloat16).reshape(reg_local, hours * columns)
    shard_rows = gather_groups(packed, "feeder", _bit_groups("feeder"))
    regions = region_map.reshape(-1)
    matches = (regions[:, None] == lax.iota(jnp.int32, total_regions)[None, :]).astype(jnp.bfloat16)
    looked = jnp.dot(matches, shard_rows, preferred_element_type=jnp.float32)
    looked = looked.reshape(ev_count, hours, columns)
    power = ev_power[0].T
    weighted = (power[:, :, None] * looked).astype(jnp.bfloat16)
    node_hot = (ev_node[0][:, :, None] == lax.iota(jnp.int32, nodes)[None, None, :]).astype(jnp.bfloat16)
    sens = sensitivity[0]
    span = hours // CHUNKS
    row_parts = []
    volts_parts = []
    variance_parts = []
    for chunk in range(CHUNKS):
        at = slice(chunk * span, (chunk + 1) * span)
        rows = jnp.einsum("hkm,mn->hkn", node_hot[at], sens, preferred_element_type=jnp.float32)
        rows = rows.astype(jnp.bfloat16)
        part = jnp.einsum("khr,hkn->hrn", weighted[:, at], rows, preferred_element_type=jnp.float32)
        row_parts.append(rows)
        volts_parts.append(part)
        variance_parts.append(sum_all(jnp.sum(part * part, axis=1), "factor"))
    factor_volts = jnp.concatenate(volts_parts, axis=0)
    sens_rows = jnp.concatenate(row_parts, axis=0)
    variance = jnp.concatenate(variance_parts, axis=0)[None]
    deviation = jnp.sqrt(variance + epsilon)
    margin = headroom - quantile * deviation
    violation = jnp.maximum(-margin, 0.0)
    var_grad = quantile * violation / deviation
    volt_grad = (2.0 * var_grad[0][:, None, :] * factor_volts).astype(jnp.bfloat16)
    picked = jnp.einsum("hkn,hrn->hkr", sens_rows, volt_grad, preferred_element_type=jnp.float32)
    picked = jnp.transpose(picked, (1, 0, 2))
    member_grads = (power[:, :, None] * picked).reshape(ev_count, hours * columns)
    grads_hi, grads_lo = _split_bf16(member_grads)
    summed = jnp.einsum("kg,kc->gc", matches, grads_hi, preferred_element_type=jnp.float32)
    summed = summed + jnp.einsum("kg,kc->gc", matches, grads_lo, preferred_element_type=jnp.float32)
    reduced = scatter_groups(summed, "feeder", _bit_groups("feeder")[::-1])
    new_loadings = loadings - step_size * reduced.reshape(reg_local, hours, columns)
    return (margin, new_loadings)


def solution(mesh):
    return jax.shard_map(
        shards,
        mesh=mesh,
        in_specs=(
            P("feeder", None, None),
            P("feeder", None, None),
            P("feeder", None, None),
            P("feeder", None, None),
            P("feeder", None),
            P("feeder", None, "factor"),
        ),
        out_specs=(P("feeder", None, None), P("feeder", None, "factor")),
        check_vma=False,
    )
```

```python
import jax
import jax.numpy as jnp
from jax import lax
from jax.sharding import PartitionSpec as P

quantile = 1.645
epsilon = 1e-06
step_size = 16.0


def _bit_count(size):
    bits = size.bit_length() - 1
    assert (1 << bits) == size
    return bits


def _exchange(x, axis, bit, size):
    perm = [(i, i ^ (1 << bit)) for i in range(size)]
    return lax.ppermute(x, axis, perm)


def gather_blocks(x, axis):
    size = lax.axis_size(axis)
    bits = _bit_count(size)
    me = lax.axis_index(axis)
    buf = x
    for step, bit in enumerate(reversed(range(bits))):
        other = _exchange(buf, axis, bit, size)
        mine = (me >> bit) & 1
        low = jnp.where(mine == 0, buf, other)
        high = jnp.where(mine == 0, other, buf)
        buf = jnp.stack([low, high], axis=step)
    return buf.reshape((size * x.shape[0],) + x.shape[1:])


def scatter_blocks(x, axis):
    size = lax.axis_size(axis)
    bits = _bit_count(size)
    me = lax.axis_index(axis)
    block = x.shape[0] // size
    buf = x.reshape((2,) * bits + (block,) + x.shape[1:])
    for bit in range(bits):
        at = bits - 1 - bit
        mine = (me >> bit) & 1
        keep = lax.dynamic_index_in_dim(buf, mine, at, keepdims=False)
        send = lax.dynamic_index_in_dim(buf, 1 - mine, at, keepdims=False)
        buf = keep + _exchange(send, axis, bit, size)
    return buf


def sum_all(x, axis):
    size = lax.axis_size(axis)
    for bit in range(_bit_count(size)):
        x = x + _exchange(x, axis, bit, size)
    return x


def _mask(j, bits):
    m = 0
    for pos, b in enumerate(bits):
        if (j >> pos) & 1:
            m |= 1 << b
    return m

def _sub(me, bits):
    s = 0
    for pos, b in enumerate(bits):
        s = s + ((me >> b) & 1) * (1 << pos)
    return s

def _send_all(x_for, axis, bits, size):
    out = {}
    for j in range(1, 1 << len(bits)):
        m = _mask(j, bits)
        out[j] = lax.ppermute(x_for(j), axis, [(i, i ^ m) for i in range(size)])
    return out

def _ordered(own, got, s, count):
    cand = jnp.stack([own] + [got[j] for j in range(1, count)])
    idx = jnp.arange(count, dtype=jnp.int32) ^ s
    return jnp.take(cand, idx, axis=0)

def gather_groups(x, axis, groups):
    size = lax.axis_size(axis)
    me = lax.axis_index(axis)
    buf = x[None]
    done = []
    for bits in groups:
        count = 1 << len(bits)
        s = _sub(me, bits)
        got = _send_all(lambda j: buf, axis, bits, size)
        stacked = _ordered(buf, got, s, count)
        buf = stacked
        done.append(bits)
    buf = buf.reshape(buf.shape[:len(groups)] + x.shape)
    order = sorted(range(len(groups)), key=lambda g: -max(groups[len(groups) - 1 - g]))
    buf = jnp.transpose(buf, order + list(range(len(groups), buf.ndim)))
    return buf.reshape((size * x.shape[0],) + x.shape[1:])

def scatter_groups(x, axis, groups):
    size = lax.axis_size(axis)
    me = lax.axis_index(axis)
    block = x.shape[0] // size
    total = sum(len(b) for b in groups)
    buf = x.reshape((2,) * total + (block,) + x.shape[1:])
    remaining = list(reversed(range(total)))
    for bits in groups:
        count = 1 << len(bits)
        s = _sub(me, bits)
        axes = [remaining.index(b) for b in reversed(bits)]
        rest = [a for a in range(len(remaining)) if a not in axes]
        buf = jnp.transpose(buf, axes + rest + list(range(len(remaining), buf.ndim)))
        buf = buf.reshape((count,) + buf.shape[len(bits):])
        remaining = [b for b in remaining if b not in bits]
        own = lax.dynamic_index_in_dim(buf, s, 0, keepdims=False)
        got = _send_all(lambda j: lax.dynamic_index_in_dim(buf, s ^ j, 0, keepdims=False), axis, bits, size)
        acc = own
        for j in range(1, count):
            acc = acc + got[j]
        buf = acc
    return buf

def sum_groups(x, axis, groups):
    size = lax.axis_size(axis)
    me = lax.axis_index(axis)
    for bits in groups:
        count = 1 << len(bits)
        s = _sub(me, bits)
        got = _send_all(lambda j: x, axis, bits, size)
        vals = _ordered(x, got, s, count)
        while vals.shape[0] > 1:
            vals = vals[0::2] + vals[1::2]
        x = vals[0]
    return x


CHUNKS = 2


def _bit_groups(axis):
    rest = list(range(1, _bit_count(lax.axis_size(axis))))
    pairs = [tuple(rest[max(0, i - 1) : i + 1]) for i in range(len(rest) - 1, -1, -2)]
    return pairs + [(0,)]


def _scatter_groups(axis):
    bits = list(range(_bit_count(lax.axis_size(axis))))
    return [tuple(bits[i : i + 2]) for i in range(0, len(bits), 2)]


def _split_bf16(x):
    high = lax.reduce_precision(x, exponent_bits=8, mantissa_bits=7)
    return high.astype(jnp.bfloat16), (x - high).astype(jnp.bfloat16)


def shards(sensitivity, headroom, ev_power, ev_node, region_map, loadings):
    reg_local, hours, columns = loadings.shape
    nodes = sensitivity.shape[2]
    ev_count = ev_power.shape[2]
    total_regions = reg_local * lax.axis_size("feeder")
    packed = loadings.astype(jnp.bfloat16).reshape(reg_local, hours * columns)
    shard_rows = gather_groups(packed, "feeder", _bit_groups("feeder"))
    regions = region_map.reshape(-1)
    matches = (regions[:, None] == lax.iota(jnp.int32, total_regions)[None, :]).astype(jnp.bfloat16)
    looked = jnp.dot(matches, shard_rows, preferred_element_type=jnp.float32)
    looked = looked.reshape(ev_count, hours, columns)
    power = ev_power[0].T
    weighted = (power[:, :, None] * looked).astype(jnp.bfloat16)
    node_hot = (ev_node[0][:, :, None] == lax.iota(jnp.int32, nodes)[None, None, :]).astype(jnp.bfloat16)
    sens = sensitivity[0]
    span = hours // CHUNKS
    row_parts = []
    volts_parts = []
    variance_parts = []
    for chunk in range(CHUNKS):
        at = slice(chunk * span, (chunk + 1) * span)
        rows = jnp.einsum("hkm,mn->hkn", node_hot[at], sens, preferred_element_type=jnp.float32)
        rows = rows.astype(jnp.bfloat16)
        part = jnp.einsum("khr,hkn->hrn", weighted[:, at], rows, preferred_element_type=jnp.float32)
        row_parts.append(rows)
        volts_parts.append(part)
        variance_parts.append(sum_all(jnp.sum(part * part, axis=1), "factor"))
    factor_volts = jnp.concatenate(volts_parts, axis=0)
    sens_rows = jnp.concatenate(row_parts, axis=0)
    variance = jnp.concatenate(variance_parts, axis=0)[None]
    deviation = jnp.sqrt(variance + epsilon)
    margin = headroom - quantile * deviation
    violation = jnp.maximum(-margin, 0.0)
    var_grad = quantile * violation / deviation
    volt_grad = (2.0 * var_grad[0][:, None, :] * factor_volts).astype(jnp.bfloat16)
    picked = jnp.einsum("hkn,hrn->khr", sens_rows, volt_grad, preferred_element_type=jnp.float32)
    member_grads = (power[:, :, None] * picked).reshape(ev_count, hours * columns)
    grads_hi, grads_lo = _split_bf16(member_grads)
    summed = jnp.einsum("kg,kc->gc", matches, grads_hi, preferred_element_type=jnp.float32)
    summed = summed + jnp.einsum("kg,kc->gc", matches, grads_lo, preferred_element_type=jnp.float32)
    reduced = scatter_groups(summed, "feeder", _scatter_groups("feeder"))
    new_loadings = loadings - step_size * reduced.reshape(reg_local, hours, columns)
    return (margin, new_loadings)


def solution(mesh):
    return jax.shard_map(
        shards,
        mesh=mesh,
        in_specs=(
            P("feeder", None, None),
            P("feeder", None, None),
            P("feeder", None, None),
            P("feeder", None, None),
            P("feeder", None),
            P("feeder", None, "factor"),
        ),
        out_specs=(P("feeder", None, None), P("feeder", None, "factor")),
        check_vma=False,
    )
```

```python
import jax
import jax.numpy as jnp
from jax import lax
from jax.sharding import PartitionSpec as P

quantile = 1.645
epsilon = 1e-06
step_size = 16.0


def _bit_count(size):
    bits = size.bit_length() - 1
    assert (1 << bits) == size
    return bits


def _exchange(x, axis, bit, size):
    perm = [(i, i ^ (1 << bit)) for i in range(size)]
    return lax.ppermute(x, axis, perm)


def gather_blocks(x, axis):
    size = lax.axis_size(axis)
    bits = _bit_count(size)
    me = lax.axis_index(axis)
    buf = x
    for step, bit in enumerate(reversed(range(bits))):
        other = _exchange(buf, axis, bit, size)
        mine = (me >> bit) & 1
        low = jnp.where(mine == 0, buf, other)
        high = jnp.where(mine == 0, other, buf)
        buf = jnp.stack([low, high], axis=step)
    return buf.reshape((size * x.shape[0],) + x.shape[1:])


def scatter_blocks(x, axis):
    size = lax.axis_size(axis)
    bits = _bit_count(size)
    me = lax.axis_index(axis)
    block = x.shape[0] // size
    buf = x.reshape((2,) * bits + (block,) + x.shape[1:])
    for bit in range(bits):
        at = bits - 1 - bit
        mine = (me >> bit) & 1
        keep = lax.dynamic_index_in_dim(buf, mine, at, keepdims=False)
        send = lax.dynamic_index_in_dim(buf, 1 - mine, at, keepdims=False)
        buf = keep + _exchange(send, axis, bit, size)
    return buf


def sum_all(x, axis):
    size = lax.axis_size(axis)
    for bit in range(_bit_count(size)):
        x = x + _exchange(x, axis, bit, size)
    return x


def _mask(j, bits):
    m = 0
    for pos, b in enumerate(bits):
        if (j >> pos) & 1:
            m |= 1 << b
    return m

def _sub(me, bits):
    s = 0
    for pos, b in enumerate(bits):
        s = s + ((me >> b) & 1) * (1 << pos)
    return s

def _send_all(x_for, axis, bits, size):
    out = {}
    for j in range(1, 1 << len(bits)):
        m = _mask(j, bits)
        out[j] = lax.ppermute(x_for(j), axis, [(i, i ^ m) for i in range(size)])
    return out

def _ordered(own, got, s, count):
    cand = jnp.stack([own] + [got[j] for j in range(1, count)])
    idx = jnp.arange(count, dtype=jnp.int32) ^ s
    return jnp.take(cand, idx, axis=0)

def gather_groups(x, axis, groups):
    size = lax.axis_size(axis)
    me = lax.axis_index(axis)
    buf = x[None]
    done = []
    for bits in groups:
        count = 1 << len(bits)
        s = _sub(me, bits)
        got = _send_all(lambda j: buf, axis, bits, size)
        stacked = _ordered(buf, got, s, count)
        buf = stacked
        done.append(bits)
    buf = buf.reshape(buf.shape[:len(groups)] + x.shape)
    order = sorted(range(len(groups)), key=lambda g: -max(groups[len(groups) - 1 - g]))
    buf = jnp.transpose(buf, order + list(range(len(groups), buf.ndim)))
    return buf.reshape((size * x.shape[0],) + x.shape[1:])

def scatter_groups(x, axis, groups):
    size = lax.axis_size(axis)
    me = lax.axis_index(axis)
    block = x.shape[0] // size
    total = sum(len(b) for b in groups)
    buf = x.reshape((2,) * total + (block,) + x.shape[1:])
    remaining = list(reversed(range(total)))
    for bits in groups:
        count = 1 << len(bits)
        s = _sub(me, bits)
        axes = [remaining.index(b) for b in reversed(bits)]
        rest = [a for a in range(len(remaining)) if a not in axes]
        buf = jnp.transpose(buf, axes + rest + list(range(len(remaining), buf.ndim)))
        buf = buf.reshape((count,) + buf.shape[len(bits):])
        remaining = [b for b in remaining if b not in bits]
        own = lax.dynamic_index_in_dim(buf, s, 0, keepdims=False)
        got = _send_all(lambda j: lax.dynamic_index_in_dim(buf, s ^ j, 0, keepdims=False), axis, bits, size)
        acc = own
        for j in range(1, count):
            acc = acc + got[j]
        buf = acc
    return buf

def sum_groups(x, axis, groups):
    size = lax.axis_size(axis)
    me = lax.axis_index(axis)
    for bits in groups:
        count = 1 << len(bits)
        s = _sub(me, bits)
        got = _send_all(lambda j: x, axis, bits, size)
        vals = _ordered(x, got, s, count)
        while vals.shape[0] > 1:
            vals = vals[0::2] + vals[1::2]
        x = vals[0]
    return x


CHUNKS = 1


def _bit_groups(axis):
    rest = list(range(1, _bit_count(lax.axis_size(axis))))
    pairs = [tuple(rest[max(0, i - 1) : i + 1]) for i in range(len(rest) - 1, -1, -2)]
    return pairs + [(0,)]


def _split_bf16(x):
    high = lax.reduce_precision(x, exponent_bits=8, mantissa_bits=7)
    return high.astype(jnp.bfloat16), (x - high).astype(jnp.bfloat16)


def shards(sensitivity, headroom, ev_power, ev_node, region_map, loadings):
    reg_local, hours, columns = loadings.shape
    nodes = sensitivity.shape[2]
    ev_count = ev_power.shape[2]
    total_regions = reg_local * lax.axis_size("feeder")
    packed = loadings.astype(jnp.bfloat16).reshape(reg_local, hours * columns)
    shard_rows = gather_groups(packed, "feeder", _bit_groups("feeder"))
    regions = region_map.reshape(-1)
    matches = (regions[:, None] == lax.iota(jnp.int32, total_regions)[None, :]).astype(jnp.bfloat16)
    looked = jnp.dot(matches, shard_rows, preferred_element_type=jnp.float32)
    looked = looked.reshape(ev_count, hours, columns)
    power = ev_power[0].T
    weighted = (power[:, :, None] * looked).astype(jnp.bfloat16)
    node_hot = (ev_node[0][:, :, None] == lax.iota(jnp.int32, nodes)[None, None, :]).astype(jnp.bfloat16)
    sens = sensitivity[0]
    span = hours // CHUNKS
    row_parts = []
    volts_parts = []
    variance_parts = []
    for chunk in range(CHUNKS):
        at = slice(chunk * span, (chunk + 1) * span)
        rows = jnp.einsum("hkm,mn->hkn", node_hot[at], sens, preferred_element_type=jnp.float32)
        rows = rows.astype(jnp.bfloat16)
        part = jnp.einsum("khr,hkn->hrn", weighted[:, at], rows, preferred_element_type=jnp.float32)
        row_parts.append(rows)
        volts_parts.append(part)
        variance_parts.append(sum_all(jnp.sum(part * part, axis=1), "factor"))
    factor_volts = jnp.concatenate(volts_parts, axis=0)
    sens_rows = jnp.concatenate(row_parts, axis=0)
    variance = jnp.concatenate(variance_parts, axis=0)[None]
    deviation = jnp.sqrt(variance + epsilon)
    margin = headroom - quantile * deviation
    violation = jnp.maximum(-margin, 0.0)
    var_grad = quantile * violation / deviation
    volt_grad = (2.0 * var_grad[0][:, None, :] * factor_volts).astype(jnp.bfloat16)
    picked = jnp.einsum("hkn,hrn->khr", sens_rows, volt_grad, preferred_element_type=jnp.float32)
    member_grads = (power[:, :, None] * picked).reshape(ev_count, hours * columns)
    grads_hi, grads_lo = _split_bf16(member_grads)
    summed = jnp.einsum("kg,kc->gc", matches, grads_hi, preferred_element_type=jnp.float32)
    summed = summed + jnp.einsum("kg,kc->gc", matches, grads_lo, preferred_element_type=jnp.float32)
    reduced = scatter_groups(summed, "feeder", _bit_groups("feeder")[::-1])
    new_loadings = loadings - step_size * reduced.reshape(reg_local, hours, columns)
    return (margin, new_loadings)


def solution(mesh):
    return jax.shard_map(
        shards,
        mesh=mesh,
        in_specs=(
            P("feeder", None, None),
            P("feeder", None, None),
            P("feeder", None, None),
            P("feeder", None, None),
            P("feeder", None),
            P("feeder", None, "factor"),
        ),
        out_specs=(P("feeder", None, None), P("feeder", None, "factor")),
        check_vma=False,
    )
```
